128 devices in a mesh: strip: 32 (over y, x, core), visit: 4 (over z).
Axes of the slice: x: 4, y: 4, z: 4, core: 2. Of those that a mesh axis runs over, the one named last changes fastest.
Arguments:
- sky_model: float32 [1024, 4096], P('strip'), may hold values from -6 to 6
- exposures: bfloat16 [16, 1024, 4096], P('visit', 'strip'), may hold values from -6 to 6
- warp_mats: bfloat16 [16, 32, 3, 128, 128], P('visit'), may hold values from -0.3125 to 0.3125
- warp_blocks: int32 [16, 32, 3], P('visit'), may hold values from 0 to 31
- psf_cols: float32 [16, 33], P('visit'), may hold values from 0 to 1, as said below
- psf_rows: float32 [16, 33], P('visit'), may hold values from 0 to 1, as said below
- bad_boxes: int32 [16, 32, 4], P('visit'), may hold values from 0 to 4096, as said below
- footprints: int32 [16, 4], P('visit'), may hold values from 0 to 4096, as said below
Outputs:
- estimate: float32 [1024, 4096], P('strip')
The draws below stay inside these ranges and needn't reach their ends.
Inputs may be any that keep to these rules, and one draw needn't show every extreme that they name: `bad_boxes`: in each rectangle the end row exceeds the first row and the end column exceeds the first column; ends are exclusive. `footprints`: each tile covers at least the middle half of the rows and of the columns; ends are exclusive. `psf_cols`: kernel taps are positive. `psf_rows`: kernel taps are positive.
All inputs are finite; a program needn't handle non-finite values.
Results may differ from the reference program's by a relative error of at most 0.0003.
Values may be sent and summed in bfloat16 or wider, within the bound.
No kernel may reach another device: no remote copies, remote signals or barrier semaphores. Data moves between devices by JAX's collectives and lax.ppermute only.
A program may use at most 128 MiB of HBM per device.

```python
import jax
import jax.numpy as jnp
from jax import lax

NC = 4096
K = 3
TAPS = 33
NBOX = 32
STEPS = 2
NR = 1024
VISITS = 16
NCB = 32


def kernel_draw(key, salt):
    center = TAPS // 2
    offsets = jnp.arange(TAPS, dtype=jnp.float32)[None, :] - center
    core = jax.random.uniform(jax.random.fold_in(key, salt + 1), (VISITS, 1), jnp.float32, 0.3, 0.6)
    sigma = jnp.exp(jax.random.uniform(jax.random.fold_in(key, salt + 2), (VISITS, 1), jnp.float32, 0.405, 1.609))
    rough = jax.random.uniform(jax.random.fold_in(key, salt + 3), (VISITS, TAPS), jnp.float32, 0.6, 1.4)
    wings = 0.4 * jnp.exp(-0.5 * (offsets / sigma) ** 2) / sigma
    floor = jax.random.uniform(jax.random.fold_in(key, salt + 4), (VISITS, TAPS), jnp.float32, 0.002, 0.008)
    peak = jnp.where(offsets == 0, core, 0.0)
    return (peak + wings * rough + floor).astype(jnp.float32)


def draw_psf_cols(key, part):
    return kernel_draw(key, 30)


def draw_psf_rows(key, part):
    return kernel_draw(key, 40)


def draw_bad_boxes(key, part):
    row_tops = jax.random.randint(jax.random.fold_in(key, 11), (VISITS, NBOX), 0, NR)
    heights = jax.random.randint(jax.random.fold_in(key, 12), (VISITS, NBOX), 1, NR // 8 + 1)
    col_lefts = jax.random.randint(jax.random.fold_in(key, 13), (VISITS, NBOX), 0, NC)
    widths = jax.random.randint(jax.random.fold_in(key, 14), (VISITS, NBOX), 1, NC // 8 + 1)
    row_ends = jnp.minimum(row_tops + heights, NR)
    col_ends = jnp.minimum(col_lefts + widths, NC)
    corner_box = (jnp.arange(NBOX) == 0)[None, :]
    row_tops = jnp.where(corner_box, NR - heights, row_tops)
    row_ends = jnp.where(corner_box, NR, row_ends)
    col_lefts = jnp.where(corner_box, NC - widths, col_lefts)
    col_ends = jnp.where(corner_box, NC, col_ends)
    return jnp.stack([row_tops, row_ends, col_lefts, col_ends], axis=-1).astype(jnp.int32)


def draw_footprints(key, part):
    keep_cut = (jnp.arange(VISITS) > 0)[:, None].astype(jnp.int32)
    row_cuts = jax.random.randint(jax.random.fold_in(key, 21), (VISITS, 2), 0, NR // 4 + 1) * keep_cut
    col_cuts = jax.random.randint(jax.random.fold_in(key, 22), (VISITS, 2), 0, NC // 4 + 1) * keep_cut
    return jnp.stack([row_cuts[:, 0], NR - row_cuts[:, 1], col_cuts[:, 0], NC - col_cuts[:, 1]], axis=-1).astype(jnp.int32)


def set_ends(array, own_key, low, largest):
    index_at = [jax.random.randint(jax.random.fold_in(own_key, axis), (), 0, length) for axis, length in enumerate(array.shape)]
    widest = array.shape.index(max(array.shape))
    beside = index_at[:widest] + [(index_at[widest] + 1) % array.shape[widest]] + index_at[widest + 1:]
    return array.at[tuple(index_at)].set(low).at[tuple(beside)].set(largest)


def block_levels(rng, extent, pieces, smallest, top_value):
    loudness = 1.0
    for axis_at, blocks in pieces:
        steps = jax.random.uniform(jax.random.fold_in(jax.random.fold_in(rng, 6), axis_at), (blocks,), jnp.float32, smallest / len(pieces), top_value / len(pieces))
        loudness = loudness * jnp.repeat(jnp.exp(steps), extent[axis_at] // blocks).reshape((-1,) + (1,) * (len(extent) - 1 - axis_at))
    return loudness


def scatter_about(own_key, extent, scale, bound, pieces=(), kind=jnp.bfloat16):
    loudness = block_levels(own_key, extent, pieces, -0.22, 0.18) if pieces else 1.0
    values = jax.random.normal(own_key, extent, jnp.float32) * scale * loudness
    return jnp.minimum(jnp.maximum(values, -bound), bound).astype(kind)


def setup_inputs(seed: int = 0) -> dict:
    key_list = jax.random.split(jax.random.key(seed), 9)
    return {
        "sky_model": scatter_about(key_list[0], (NR, NC), 1.0, 6.0, ((0, 32),), jnp.float32),
        "exposures": scatter_about(key_list[1], (VISITS, NR, NC), 1.0, 6.0, ((0, 4), (1, 32))),
        "warp_mats": scatter_about(key_list[2], (VISITS, NCB, K, 128, 128), (128 * K) ** -0.5, 0.3125, ((0, 4),)),
        "warp_blocks": set_ends(jax.random.randint(key_list[3], (VISITS, NCB, K), 0, NCB), jax.random.fold_in(key_list[3], 1), 0, NCB - 1).astype(jnp.int32),
        "psf_cols": draw_psf_cols(jax.random.fold_in(key_list[8], 71), 0),
        "psf_rows": draw_psf_rows(jax.random.fold_in(key_list[8], 71), 0),
        "bad_boxes": draw_bad_boxes(jax.random.fold_in(key_list[8], 71), 0),
        "footprints": draw_footprints(jax.random.fold_in(key_list[8], 71), 0),
    }


precise = lax.Precision.HIGHEST


def conv_rows(image_in, kernel):
    margin = kernel.shape[0] // 2
    padded = jnp.pad(image_in, ((margin, margin), (0, 0)))
    running = jnp.zeros(image_in.shape, jnp.float32)
    for tap_index in range(kernel.shape[0]):
        running = running + kernel[tap_index] * padded[tap_index:tap_index + image_in.shape[0], :]
    return running


def conv_cols(image_in, kernel):
    margin = kernel.shape[0] // 2
    padded = jnp.pad(image_in, ((0, 0), (margin, margin)))
    running = jnp.zeros(image_in.shape, jnp.float32)
    for tap_index in range(kernel.shape[0]):
        running = running + kernel[tap_index] * padded[:, tap_index:tap_index + image_in.shape[1]]
    return running


def warp_forward(image_in, matrices, sources):
    blocks = image_in.reshape(NR, NCB, 128)
    picked = blocks[:, sources]
    mapped = jnp.einsum("rjki,jkio->rjo", picked, matrices.astype(jnp.float32), precision=precise)
    return mapped.reshape(NR, NC)


def warp_adjoint(image_in, matrices, sources):
    blocks = image_in.reshape(NR, NCB, 128)
    spread = jnp.einsum("rjo,jkio->rjki", blocks, matrices.astype(jnp.float32), precision=precise)
    onehot = (sources[:, :, None] == jnp.arange(NCB, dtype=jnp.int32)[None, None, :]).astype(jnp.float32)
    folded = jnp.einsum("rjki,jkb->rbi", spread, onehot, precision=precise)
    return folded.reshape(NR, NC)


def mask_of(row_ids, col_ids, bad_list, footprint):
    row_hits = ((row_ids[None, :] >= bad_list[:, 0:1]) & (row_ids[None, :] < bad_list[:, 1:2])).astype(jnp.float32)
    col_hits = ((col_ids[None, :] >= bad_list[:, 2:3]) & (col_ids[None, :] < bad_list[:, 3:4])).astype(jnp.float32)
    covered = jnp.dot(row_hits.T, col_hits, preferred_element_type=jnp.float32)
    inside_rows = ((row_ids >= footprint[0]) & (row_ids < footprint[1])).astype(jnp.float32)
    inside_cols = ((col_ids >= footprint[2]) & (col_ids < footprint[3])).astype(jnp.float32)
    return jnp.where(covered > 0.5, 0.0, 1.0).astype(jnp.float32) * inside_rows[:, None] * inside_cols[None, :]


def reference(sky_model, exposures, warp_mats, warp_blocks, psf_cols, psf_rows, bad_boxes, footprints):
    row_ids = jnp.arange(NR, dtype=jnp.int32)
    col_ids = jnp.arange(NC, dtype=jnp.int32)
    visit_list = jnp.arange(VISITS, dtype=jnp.int32)

    def forward(image_in, visit_index):
        warped = warp_forward(image_in, warp_mats[visit_index], warp_blocks[visit_index])
        blurred = conv_cols(warped, psf_cols[visit_index])
        blurred = conv_rows(blurred, psf_rows[visit_index])
        return mask_of(row_ids, col_ids, bad_boxes[visit_index], footprints[visit_index]) * blurred

    def first_residual(visit_index):
        masked = mask_of(row_ids, col_ids, bad_boxes[visit_index], footprints[visit_index])
        return forward(sky_model, visit_index) - masked * exposures[visit_index].astype(jnp.float32)

    residuals = lax.map(first_residual, visit_list)
    estimate = sky_model
    for step_index in range(STEPS):
        def accumulate(carry, visit_index):
            back_rows = conv_rows(residuals[visit_index], psf_rows[visit_index][::-1])
            back_cols = conv_cols(back_rows, psf_cols[visit_index][::-1])
            return carry + warp_adjoint(back_cols, warp_mats[visit_index], warp_blocks[visit_index]), None

        gradient, unused = lax.scan(accumulate, jnp.zeros((NR, NC), jnp.float32), visit_list)
        images = lax.map(lambda visit_index: forward(gradient, visit_index), visit_list)
        step_size = jnp.sum(gradient * gradient) / jnp.sum(images * images)
        estimate = estimate - step_size * gradient
        residuals = residuals - step_size * images
    return estimate
```

```python
import jax
import jax.numpy as jnp
from jax import lax
from jax.sharding import PartitionSpec as P

STEPS = 2

f32 = jnp.float32
bf16 = jnp.bfloat16


def split(a):
    hi = lax.reduce_precision(a, exponent_bits=8, mantissa_bits=7)
    return hi.astype(bf16), (a - hi).astype(bf16)


def mm(eq, a, b):
    return jnp.einsum(eq, a, b, preferred_element_type=f32)


def dot3(eq, a, b):
    a_hi, a_lo = split(a)
    b_hi, b_lo = split(b)
    return mm(eq, a_hi, b_hi) + (mm(eq, a_hi, b_lo) + mm(eq, a_lo, b_hi))


def dot2(eq, a, b_exact):
    a_hi, a_lo = split(a)
    return mm(eq, a_hi, b_exact) + mm(eq, a_lo, b_exact)


def mask_of(row_ids, col_ids, bad_list, footprint):
    row_hits = (
        (row_ids[None, :] >= bad_list[:, 0:1]) & (row_ids[None, :] < bad_list[:, 1:2])
    ).astype(f32)
    col_hits = (
        (col_ids[None, :] >= bad_list[:, 2:3]) & (col_ids[None, :] < bad_list[:, 3:4])
    ).astype(f32)
    covered = jnp.dot(row_hits.T, col_hits, preferred_element_type=f32)
    inside_rows = ((row_ids >= footprint[0]) & (row_ids < footprint[1])).astype(f32)
    inside_cols = ((col_ids >= footprint[2]) & (col_ids < footprint[3])).astype(f32)
    return (
        jnp.where(covered > 0.5, 0.0, 1.0).astype(f32)
        * inside_rows[:, None]
        * inside_cols[None, :]
    )


def local(sky_model, exposures, warp_mats, warp_blocks, psf_cols, psf_rows, bad_boxes, footprints):
    strips = lax.axis_size("strip")
    strip_index = lax.axis_index("strip")
    rows = sky_model.shape[0]
    columns = sky_model.shape[1]
    nb = columns // 128
    visits_here = warp_mats.shape[0]
    taps = psf_cols.shape[1]
    margin = taps // 2
    ext = rows + 2 * margin

    r_id = jnp.arange(rows)[:, None]
    e_id = jnp.arange(ext)[None, :]
    t_id = e_id - r_id
    row_band = jnp.where(
        (t_id >= 0) & (t_id < taps), psf_rows[:, jnp.clip(t_id, 0, taps - 1)], 0.0
    )

    d_id = jnp.arange(3)[:, None, None] - 1
    i_id = jnp.arange(128)[None, :, None]
    o_id = jnp.arange(128)[None, None, :]
    c_t = 128 * d_id + i_id - o_id + margin
    col_band = jnp.where(
        (c_t >= 0) & (c_t < taps), psf_cols[:, jnp.clip(c_t, 0, taps - 1)], 0.0
    )
    col_band_t = jnp.swapaxes(col_band, 2, 3)

    onehot = (warp_blocks[..., None] == jnp.arange(nb, dtype=jnp.int32)).astype(bf16)

    row_ids = strip_index * rows + jnp.arange(rows, dtype=jnp.int32)
    col_ids = jnp.arange(columns, dtype=jnp.int32)
    pixel_masks = jax.vmap(mask_of, in_axes=(None, None, 0, 0))(
        row_ids, col_ids, bad_boxes, footprints
    )

    up = [(s, s - 1) for s in range(1, strips)]
    down = [(s, s + 1) for s in range(strips - 1)]

    def with_halo(x):
        above = lax.ppermute(x[rows - margin:], "strip", down)
        below = lax.ppermute(x[:margin], "strip", up)
        return jnp.concatenate([above, x, below], axis=0)

    def shift_blocks(y, d):
        if d == 0:
            return y
        zeros = jnp.zeros_like(y[..., :1, :])
        if d > 0:
            return jnp.concatenate([y[..., d:, :], zeros], axis=-2)
        return jnp.concatenate([zeros, y[..., :d, :]], axis=-2)

    def forward(x_ext):
        blurred_rows = dot3("vre,ec->vrc", row_band, x_ext)
        hi, lo = split(blurred_rows)
        hi = hi.reshape(visits_here, rows, nb, 128)
        lo = lo.reshape(visits_here, rows, nb, 128)
        pick = jax.vmap(lambda u, wb: u[:, wb])
        warped = mm("vrjki,vjkio->vrjo", pick(hi, warp_blocks), warp_mats) + mm(
            "vrjki,vjkio->vrjo", pick(lo, warp_blocks), warp_mats
        )
        out = None
        for d in range(3):
            term = dot3("vrji,vio->vrjo", shift_blocks(warped, d - 1), col_band[:, d])
            out = term if out is None else out + term
        return pixel_masks * out.reshape(visits_here, rows, columns)

    def adjoint_partial(res):
        z = res.reshape(visits_here, rows, nb, 128)
        back = None
        for d in range(3):
            term = dot3("vrji,vio->vrjo", shift_blocks(z, 1 - d), col_band_t[:, d])
            back = term if back is None else back + term
        spread = dot2("vrjo,vjkio->vrjki", back, warp_mats)
        folded = dot2("vrjki,vjkb->vrbi", spread, onehot)
        folded = folded.reshape(visits_here, rows, columns)
        return dot3("vre,vrc->ec", row_band, folded)

    def reduce_partial(part):
        from_below = lax.ppermute(part[ext - margin:], "strip", down)
        from_above = lax.ppermute(part[:margin], "strip", up)
        mid = part[margin:margin + rows]
        mid = mid + jnp.concatenate(
            [from_below, jnp.zeros((rows - margin, columns), f32)], axis=0
        )
        mid = mid + jnp.concatenate(
            [jnp.zeros((rows - margin, columns), f32), from_above], axis=0
        )
        return lax.psum(mid, "visit")

    observed = exposures.astype(f32)
    estimate = sky_model
    residual = forward(with_halo(sky_model)) - pixel_masks * observed
    for step_index in range(STEPS):
        gradient = reduce_partial(adjoint_partial(residual))
        image_grad = forward(with_halo(gradient))
        grad_total, curvature = lax.psum(
            (jnp.sum(gradient * gradient) / lax.axis_size("visit"), jnp.sum(image_grad * image_grad)),
            ("strip", "visit"),
        )
        step_size = grad_total / curvature
        estimate = estimate - step_size * gradient
        residual = residual - step_size * image_grad
    return estimate


def solution(mesh):
    return jax.shard_map(
        local,
        mesh=mesh,
        in_specs=(
            P("strip", None),
            P("visit", "strip", None),
            P("visit", None, None, None, None),
            P("visit", None, None),
            P("visit", None),
            P("visit", None),
            P("visit", None, None),
            P("visit", None),
        ),
        out_specs=P("strip", None),
        check_vma=False,
    )
```

```python
import jax
import jax.numpy as jnp
from jax import lax
from jax.sharding import PartitionSpec as P

STEPS = 2

f32 = jnp.float32
bf16 = jnp.bfloat16


def split(a):
    hi = lax.reduce_precision(a, exponent_bits=8, mantissa_bits=7)
    return hi.astype(bf16), (a - hi).astype(bf16)


def mm(eq, a, b):
    return jnp.einsum(eq, a, b, preferred_element_type=f32)


def dot3(eq, a, b):
    a_hi, a_lo = split(a)
    b_hi, b_lo = split(b)
    return mm(eq, a_hi, b_hi) + (mm(eq, a_hi, b_lo) + mm(eq, a_lo, b_hi))


def dot2(eq, a, b_exact):
    a_hi, a_lo = split(a)
    return mm(eq, a_hi, b_exact) + mm(eq, a_lo, b_exact)


def xor_pairs(n, bit):
    return [(i, i ^ bit) for i in range(n)]


def all_sum(x, axis, n, lowest=1):
    bit = lowest
    while bit < n:
        if 2 * bit < n:
            near = x + lax.ppermute(x, axis, xor_pairs(n, bit))
            far = lax.ppermute(x, axis, xor_pairs(n, 2 * bit)) + lax.ppermute(
                x, axis, xor_pairs(n, 3 * bit)
            )
            x = near + far
            bit *= 4
        else:
            x = x + lax.ppermute(x, axis, xor_pairs(n, bit))
            bit *= 2
    return x


def mask_of(row_ids, col_ids, bad_list, footprint):
    row_hits = (
        (row_ids[None, :] >= bad_list[:, 0:1]) & (row_ids[None, :] < bad_list[:, 1:2])
    ).astype(f32)
    col_hits = (
        (col_ids[None, :] >= bad_list[:, 2:3]) & (col_ids[None, :] < bad_list[:, 3:4])
    ).astype(f32)
    covered = jnp.dot(row_hits.T, col_hits, preferred_element_type=f32)
    inside_rows = ((row_ids >= footprint[0]) & (row_ids < footprint[1])).astype(f32)
    inside_cols = ((col_ids >= footprint[2]) & (col_ids < footprint[3])).astype(f32)
    return (
        jnp.where(covered > 0.5, 0.0, 1.0).astype(f32)
        * inside_rows[:, None]
        * inside_cols[None, :]
    )


def local(sky_model, exposures, warp_mats, warp_blocks, psf_cols, psf_rows, bad_boxes, footprints):
    strips = lax.axis_size("strip")
    strip_index = lax.axis_index("strip")
    rows = sky_model.shape[0]
    columns = sky_model.shape[1]
    nb = columns // 128
    visits_here = warp_mats.shape[0]
    taps = psf_cols.shape[1]
    margin = taps // 2
    ext = rows + 2 * margin

    r_id = jnp.arange(rows)[:, None]
    e_id = jnp.arange(ext)[None, :]
    t_id = e_id - r_id
    row_band = sum(
        jnp.where(t_id == t, psf_rows[:, t, None, None], 0.0) for t in range(taps)
    )

    d_id = jnp.arange(3)[:, None, None] - 1
    i_id = jnp.arange(128)[None, :, None]
    o_id = jnp.arange(128)[None, None, :]
    c_t = 128 * d_id + i_id - o_id + margin
    col_band = sum(
        jnp.where(c_t == t, psf_cols[:, t, None, None, None], 0.0) for t in range(taps)
    )
    col_band_t = jnp.swapaxes(col_band, 2, 3)

    onehot = (warp_blocks[..., None] == jnp.arange(nb, dtype=jnp.int32)).astype(bf16)

    row_ids = strip_index * rows + jnp.arange(rows, dtype=jnp.int32)
    col_ids = jnp.arange(columns, dtype=jnp.int32)
    pixel_masks = jax.vmap(mask_of, in_axes=(None, None, 0, 0))(
        row_ids, col_ids, bad_boxes, footprints
    )

    up = [(s, s - 1) for s in range(1, strips)]
    down = [(s, s + 1) for s in range(strips - 1)]

    def with_halo(x):
        above = lax.ppermute(x[rows - margin:], "strip", down)
        below = lax.ppermute(x[:margin], "strip", up)
        return jnp.concatenate([above, x, below], axis=0)

    def shift_blocks(y, d):
        if d == 0:
            return y
        zeros = jnp.zeros_like(y[..., :1, :])
        if d > 0:
            return jnp.concatenate([y[..., d:, :], zeros], axis=-2)
        return jnp.concatenate([zeros, y[..., :d, :]], axis=-2)

    def forward(x_ext):
        blurred_rows = dot3("vre,ec->vrc", row_band, x_ext)
        hi, lo = split(blurred_rows)
        hi = hi.reshape(visits_here, rows, nb, 128)
        lo = lo.reshape(visits_here, rows, nb, 128)
        pick = jax.vmap(lambda u, wb: u[:, wb])
        warped = mm("vrjki,vjkio->vrjo", pick(hi, warp_blocks), warp_mats) + mm(
            "vrjki,vjkio->vrjo", pick(lo, warp_blocks), warp_mats
        )
        out = None
        for d in range(3):
            term = dot3("vrji,vio->vrjo", shift_blocks(warped, d - 1), col_band[:, d])
            out = term if out is None else out + term
        return pixel_masks * out.reshape(visits_here, rows, columns)

    def adjoint_partial(res):
        z = res.reshape(visits_here, rows, nb, 128)
        back = None
        for d in range(3):
            term = dot3("vrji,vio->vrjo", shift_blocks(z, 1 - d), col_band_t[:, d])
            back = term if back is None else back + term
        spread = dot2("vrjo,vjkio->vrjki", back, warp_mats)
        folded = dot2("vrjki,vjkb->vrbi", spread, onehot)
        folded = folded.reshape(visits_here, rows, columns)
        return dot3("vre,vrc->ec", row_band, folded)

    def reduce_partial(part):
        from_below = lax.ppermute(part[ext - margin:], "strip", down)
        from_above = lax.ppermute(part[:margin], "strip", up)
        mid = part[margin:margin + rows]
        mid = mid + jnp.concatenate(
            [from_below, jnp.zeros((rows - margin, columns), f32)], axis=0
        )
        mid = mid + jnp.concatenate(
            [jnp.zeros((rows - margin, columns), f32), from_above], axis=0
        )
        return all_sum(mid, "visit", lax.axis_size("visit"))

    observed = exposures.astype(f32)
    estimate = sky_model
    residual = forward(with_halo(sky_model)) - pixel_masks * observed
    for step_index in range(STEPS):
        gradient = reduce_partial(adjoint_partial(residual))
        image_grad = forward(with_halo(gradient))
        sums = jnp.stack(
            [
                jnp.sum(gradient * gradient),
                all_sum(jnp.sum(image_grad * image_grad), "visit", lax.axis_size("visit")),
            ]
        )
        grad_total, curvature = all_sum(sums, "strip", strips)
        step_size = grad_total / curvature
        estimate = estimate - step_size * gradient
        residual = residual - step_size * image_grad
    return estimate


def solution(mesh):
    return jax.shard_map(
        local,
        mesh=mesh,
        in_specs=(
            P("strip", None),
            P("visit", "strip", None),
            P("visit", None, None, None, None),
            P("visit", None, None),
            P("visit", None),
            P("visit", None),
            P("visit", None, None),
            P("visit", None),
        ),
        out_specs=P("strip", None),
        check_vma=False,
    )
```

```python
import jax
import jax.numpy as jnp
from jax import lax
from jax.sharding import PartitionSpec as P

STEPS = 2

f32 = jnp.float32
bf16 = jnp.bfloat16


def split(a):
    hi = lax.reduce_precision(a, exponent_bits=8, mantissa_bits=7)
    return hi.astype(bf16), (a - hi).astype(bf16)


def mm(eq, a, b):
    return jnp.einsum(eq, a, b, preferred_element_type=f32)


def dot3(eq, a, b):
    a_hi, a_lo = split(a)
    b_hi, b_lo = split(b)
    return mm(eq, a_hi, b_hi) + (mm(eq, a_hi, b_lo) + mm(eq, a_lo, b_hi))


def dot2(eq, a, b_exact):
    a_hi, a_lo = split(a)
    return mm(eq, a_hi, b_exact) + mm(eq, a_lo, b_exact)


def xor_pairs(n, bit):
    return [(i, i ^ bit) for i in range(n)]


def all_sum(x, axis, n, lowest=1):
    bit = lowest
    while bit < n:
        if 2 * bit < n:
            near = x + lax.ppermute(x, axis, xor_pairs(n, bit))
            far = lax.ppermute(x, axis, xor_pairs(n, 2 * bit)) + lax.ppermute(
                x, axis, xor_pairs(n, 3 * bit)
            )
            x = near + far
            bit *= 4
        else:
            x = x + lax.ppermute(x, axis, xor_pairs(n, bit))
            bit *= 2
    return x


def mask_of(row_ids, col_ids, bad_list, footprint):
    row_hits = (
        (row_ids[None, :] >= bad_list[:, 0:1]) & (row_ids[None, :] < bad_list[:, 1:2])
    ).astype(f32)
    col_hits = (
        (col_ids[None, :] >= bad_list[:, 2:3]) & (col_ids[None, :] < bad_list[:, 3:4])
    ).astype(f32)
    covered = jnp.dot(row_hits.T, col_hits, preferred_element_type=f32)
    inside_rows = ((row_ids >= footprint[0]) & (row_ids < footprint[1])).astype(f32)
    inside_cols = ((col_ids >= footprint[2]) & (col_ids < footprint[3])).astype(f32)
    return (
        jnp.where(covered > 0.5, 0.0, 1.0).astype(f32)
        * inside_rows[:, None]
        * inside_cols[None, :]
    )


def local(sky_model, exposures, warp_mats, warp_blocks, psf_cols, psf_rows, bad_boxes, footprints):
    strips = lax.axis_size("strip")
    strip_index = lax.axis_index("strip")
    rows = sky_model.shape[0]
    columns = sky_model.shape[1]
    nb = columns // 128
    visits_here = warp_mats.shape[0]
    taps = psf_cols.shape[1]
    margin = taps // 2
    ext = rows + 2 * margin

    r_id = jnp.arange(rows)[:, None]
    e_id = jnp.arange(ext)[None, :]
    t_id = e_id - r_id
    row_band = sum(
        jnp.where(t_id == t, psf_rows[:, t, None, None], 0.0) for t in range(taps)
    )

    d_id = jnp.arange(3)[:, None, None] - 1
    i_id = jnp.arange(128)[None, :, None]
    o_id = jnp.arange(128)[None, None, :]
    c_t = 128 * d_id + i_id - o_id + margin
    col_band = sum(
        jnp.where(c_t == t, psf_cols[:, t, None, None, None], 0.0) for t in range(taps)
    )
    col_band_t = jnp.swapaxes(col_band, 2, 3)

    onehot = (warp_blocks[..., None] == jnp.arange(nb, dtype=jnp.int32)).astype(bf16)

    row_ids = strip_index * rows + jnp.arange(rows, dtype=jnp.int32)
    col_ids = jnp.arange(columns, dtype=jnp.int32)
    pixel_masks = jax.vmap(mask_of, in_axes=(None, None, 0, 0))(
        row_ids, col_ids, bad_boxes, footprints
    )

    up = [(s, s - 1) for s in range(1, strips)]
    down = [(s, s + 1) for s in range(strips - 1)]

    def with_halo(x):
        above = lax.ppermute(x[rows - margin:], "strip", down)
        below = lax.ppermute(x[:margin], "strip", up)
        return jnp.concatenate([above, x, below], axis=0)

    def shift_blocks(y, d):
        if d == 0:
            return y
        zeros = jnp.zeros_like(y[..., :1, :])
        if d > 0:
            return jnp.concatenate([y[..., d:, :], zeros], axis=-2)
        return jnp.concatenate([zeros, y[..., :d, :]], axis=-2)

    def forward(x_ext):
        blurred_rows = dot3("vre,ec->vrc", row_band, x_ext)
        both = jnp.concatenate(split(blurred_rows), axis=1)
        both = both.reshape(visits_here, 2 * rows, nb, 128)
        pick = jax.vmap(lambda u, wb: u[:, wb])
        warped = mm("vrjki,vjkio->vrjo", pick(both, warp_blocks), warp_mats)
        warped = warped[:, :rows] + warped[:, rows:]
        out = None
        for d in range(3):
            term = dot3("vrji,vio->vrjo", shift_blocks(warped, d - 1), col_band[:, d])
            out = term if out is None else out + term
        return pixel_masks * out.reshape(visits_here, rows, columns)

    def adjoint_partial(res):
        z = res.reshape(visits_here, rows, nb, 128)
        back = None
        for d in range(3):
            term = dot3("vrji,vio->vrjo", shift_blocks(z, 1 - d), col_band_t[:, d])
            back = term if back is None else back + term
        spread = mm("vrjo,vjkio->vrjki", jnp.concatenate(split(back), axis=1), warp_mats)
        spread = spread[:, :rows] + spread[:, rows:]
        folded = mm("vrjki,vjkb->vrbi", jnp.concatenate(split(spread), axis=1), onehot)
        folded = folded[:, :rows] + folded[:, rows:]
        folded = folded.reshape(visits_here, rows, columns)
        return dot3("vre,vrc->ec", row_band, folded)

    visit_count = lax.axis_size("visit")
    visit_index = lax.axis_index("visit")

    def visit_sum(x):
        pieces = x.reshape(rows, visit_count, columns // visit_count).swapaxes(0, 1)
        own = pieces[visit_index]
        got = []
        for d in range(1, visit_count):
            send = lax.dynamic_index_in_dim(pieces, visit_index ^ d, 0, keepdims=False)
            got.append(lax.ppermute(send, "visit", xor_pairs(visit_count, d)))
        own = (own + got[0]) + (got[1] + got[2]) if visit_count == 4 else own + sum(got)
        gathered = [own] + [
            lax.ppermute(own, "visit", xor_pairs(visit_count, d)) for d in range(1, visit_count)
        ]
        order = jnp.arange(visit_count) ^ visit_index
        full = jnp.stack(gathered)[order]
        return full.swapaxes(0, 1).reshape(rows, columns)

    def reduce_partial(part):
        from_below = lax.ppermute(part[ext - margin:], "strip", down)
        from_above = lax.ppermute(part[:margin], "strip", up)
        mid = part[margin:margin + rows]
        mid = mid + jnp.concatenate(
            [from_below, jnp.zeros((rows - margin, columns), f32)], axis=0
        )
        mid = mid + jnp.concatenate(
            [jnp.zeros((rows - margin, columns), f32), from_above], axis=0
        )
        return visit_sum(mid)

    observed = exposures.astype(f32)
    estimate = sky_model
    residual = forward(with_halo(sky_model)) - pixel_masks * observed
    for step_index in range(STEPS):
        gradient = reduce_partial(adjoint_partial(residual))
        image_grad = forward(with_halo(gradient))
        sums = jnp.stack(
            [
                jnp.sum(gradient * gradient),
                all_sum(jnp.sum(image_grad * image_grad), "visit", lax.axis_size("visit")),
            ]
        )
        grad_total, curvature = all_sum(sums, "strip", strips)
        step_size = grad_total / curvature
        estimate = estimate - step_size * gradient
        residual = residual - step_size * image_grad
    return estimate


def solution(mesh):
    return jax.shard_map(
        local,
        mesh=mesh,
        in_specs=(
            P("strip", None),
            P("visit", "strip", None),
            P("visit", None, None, None, None),
            P("visit", None, None),
            P("visit", None),
            P("visit", None),
            P("visit", None, None),
            P("visit", None),
        ),
        out_specs=P("strip", None),
        check_vma=False,
    )
```

```python
import jax
import jax.numpy as jnp
from jax import lax
from jax.sharding import PartitionSpec as P

STEPS = 2

f32 = jnp.float32
bf16 = jnp.bfloat16


def split(a):
    hi = lax.reduce_precision(a, exponent_bits=8, mantissa_bits=7)
    return hi.astype(bf16), (a - hi).astype(bf16)


def mm(eq, a, b):
    return jnp.einsum(eq, a, b, preferred_element_type=f32)


def dot3(eq, a, b):
    a_hi, a_lo = split(a)
    b_hi, b_lo = split(b)
    return mm(eq, a_hi, b_hi) + (mm(eq, a_hi, b_lo) + mm(eq, a_lo, b_hi))


def dot2(eq, a, b_exact):
    a_hi, a_lo = split(a)
    return mm(eq, a_hi, b_exact) + mm(eq, a_lo, b_exact)


def xor_pairs(n, bit):
    return [(i, i ^ bit) for i in range(n)]


def all_sum(x, axis, n, radix=4):
    bit = 1
    while bit < n:
        r = min(radix, n // bit)
        vals = [x] + [lax.ppermute(x, axis, xor_pairs(n, d * bit)) for d in range(1, r)]
        while len(vals) > 1:
            vals = [vals[i] + vals[i + 1] for i in range(0, len(vals), 2)]
        x = vals[0]
        bit *= r
    return x


def mask_of(row_ids, col_ids, bad_list, footprint):
    row_hits = (
        (row_ids[None, :] >= bad_list[:, 0:1]) & (row_ids[None, :] < bad_list[:, 1:2])
    ).astype(f32)
    col_hits = (
        (col_ids[None, :] >= bad_list[:, 2:3]) & (col_ids[None, :] < bad_list[:, 3:4])
    ).astype(f32)
    covered = jnp.dot(row_hits.T, col_hits, preferred_element_type=f32)
    inside_rows = ((row_ids >= footprint[0]) & (row_ids < footprint[1])).astype(f32)
    inside_cols = ((col_ids >= footprint[2]) & (col_ids < footprint[3])).astype(f32)
    return (
        jnp.where(covered > 0.5, 0.0, 1.0).astype(f32)
        * inside_rows[:, None]
        * inside_cols[None, :]
    )


def local(sky_model, exposures, warp_mats, warp_blocks, psf_cols, psf_rows, bad_boxes, footprints):
    strips = lax.axis_size("strip")
    strip_index = lax.axis_index("strip")
    rows = sky_model.shape[0]
    columns = sky_model.shape[1]
    nb = columns // 128
    visits_here = warp_mats.shape[0]
    taps = psf_cols.shape[1]
    margin = taps // 2
    ext = rows + 2 * margin

    r_id = jnp.arange(rows)[:, None]
    e_id = jnp.arange(ext)[None, :]
    t_id = e_id - r_id
    row_band = sum(
        jnp.where(t_id == t, psf_rows[:, t, None, None], 0.0) for t in range(taps)
    )

    d_id = jnp.arange(3)[:, None, None] - 1
    i_id = jnp.arange(128)[None, :, None]
    o_id = jnp.arange(128)[None, None, :]
    c_t = 128 * d_id + i_id - o_id + margin
    col_band = sum(
        jnp.where(c_t == t, psf_cols[:, t, None, None, None], 0.0) for t in range(taps)
    )
    col_band_t = jnp.swapaxes(col_band, 2, 3)

    onehot = (warp_blocks[..., None] == jnp.arange(nb, dtype=jnp.int32)).astype(bf16)

    row_ids = strip_index * rows + jnp.arange(rows, dtype=jnp.int32)
    col_ids = jnp.arange(columns, dtype=jnp.int32)
    pixel_masks = jax.vmap(mask_of, in_axes=(None, None, 0, 0))(
        row_ids, col_ids, bad_boxes, footprints
    )

    up = [(s, s - 1) for s in range(1, strips)]
    down = [(s, s + 1) for s in range(strips - 1)]

    def with_halo(x):
        above = lax.ppermute(x[rows - margin:], "strip", down)
        below = lax.ppermute(x[:margin], "strip", up)
        return jnp.concatenate([above, x, below], axis=0)

    def shift_blocks(y, d):
        if d == 0:
            return y
        zeros = jnp.zeros_like(y[..., :1, :])
        if d > 0:
            return jnp.concatenate([y[..., d:, :], zeros], axis=-2)
        return jnp.concatenate([zeros, y[..., :d, :]], axis=-2)

    def forward(x_ext):
        blurred_rows = dot3("vre,ec->vrc", row_band, x_ext)
        both = jnp.concatenate(split(blurred_rows), axis=1)
        both = both.reshape(visits_here, 2 * rows, nb, 128)
        pick = jax.vmap(lambda u, wb: u[:, wb])
        warped = mm("vrjki,vjkio->vrjo", pick(both, warp_blocks), warp_mats)
        warped = warped[:, :rows] + warped[:, rows:]
        out = None
        for d in range(3):
            term = dot3("vrji,vio->vrjo", shift_blocks(warped, d - 1), col_band[:, d])
            out = term if out is None else out + term
        return pixel_masks * out.reshape(visits_here, rows, columns)

    def adjoint_partial(res):
        z = res.reshape(visits_here, rows, nb, 128)
        back = None
        for d in range(3):
            term = dot3("vrji,vio->vrjo", shift_blocks(z, 1 - d), col_band_t[:, d])
            back = term if back is None else back + term
        spread = mm("vrjo,vjkio->vrjki", jnp.concatenate(split(back), axis=1), warp_mats)
        spread = spread[:, :rows] + spread[:, rows:]
        folded = mm("vrjki,vjkb->vrbi", jnp.concatenate(split(spread), axis=1), onehot)
        folded = folded[:, :rows] + folded[:, rows:]
        folded = folded.reshape(visits_here, rows, columns)
        return dot3("vre,vrc->ec", row_band, folded)

    visit_count = lax.axis_size("visit")
    visit_index = lax.axis_index("visit")

    def visit_sum(x):
        pieces = x.reshape(rows, visit_count, columns // visit_count).swapaxes(0, 1)
        own = pieces[visit_index]
        got = []
        for d in range(1, visit_count):
            send = lax.dynamic_index_in_dim(pieces, visit_index ^ d, 0, keepdims=False)
            got.append(lax.ppermute(send, "visit", xor_pairs(visit_count, d)))
        own = (own + got[0]) + (got[1] + got[2]) if visit_count == 4 else own + sum(got)
        gathered = [own] + [
            lax.ppermute(own, "visit", xor_pairs(visit_count, d)) for d in range(1, visit_count)
        ]
        order = jnp.arange(visit_count) ^ visit_index
        full = jnp.stack(gathered)[order]
        return full.swapaxes(0, 1).reshape(rows, columns)

    def reduce_partial(part):
        from_below = lax.ppermute(part[ext - margin:], "strip", down)
        from_above = lax.ppermute(part[:margin], "strip", up)
        mid = part[margin:margin + rows]
        mid = mid + jnp.concatenate(
            [from_below, jnp.zeros((rows - margin, columns), f32)], axis=0
        )
        mid = mid + jnp.concatenate(
            [jnp.zeros((rows - margin, columns), f32), from_above], axis=0
        )
        return visit_sum(mid)

    observed = exposures.astype(f32)
    residual = forward(with_halo(sky_model)) - pixel_masks * observed
    gradient = with_halo(reduce_partial(adjoint_partial(residual)))
    estimate = sky_model
    for step_index in range(STEPS):
        image_grad = forward(gradient)
        mid = gradient[margin:margin + rows]
        sums = jnp.stack(
            [
                jnp.sum(mid * mid),
                all_sum(jnp.sum(image_grad * image_grad), "visit", lax.axis_size("visit")),
            ]
        )
        grad_total, curvature = all_sum(sums, "strip", strips, radix=8)
        step_size = grad_total / curvature
        estimate = estimate - step_size * mid
        if step_index + 1 < STEPS:
            normal = with_halo(reduce_partial(adjoint_partial(image_grad)))
            gradient = gradient - step_size * normal
    return estimate


def solution(mesh):
    return jax.shard_map(
        local,
        mesh=mesh,
        in_specs=(
            P("strip", None),
            P("visit", "strip", None),
            P("visit", None, None, None, None),
            P("visit", None, None),
            P("visit", None),
            P("visit", None),
            P("visit", None, None),
            P("visit", None),
        ),
        out_specs=P("strip", None),
        check_vma=False,
    )
```

```python
import jax
import jax.numpy as jnp
from jax import lax
from jax.sharding import PartitionSpec as P

STEPS = 2

f32 = jnp.float32
bf16 = jnp.bfloat16


def split(a):
    hi = lax.reduce_precision(a, exponent_bits=8, mantissa_bits=7)
    return hi.astype(bf16), (a - hi).astype(bf16)


def mm(eq, a, b):
    return jnp.einsum(eq, a, b, preferred_element_type=f32)


def dot3(eq, a, b):
    a_hi, a_lo = split(a)
    b_hi, b_lo = split(b)
    return mm(eq, a_hi, b_hi) + (mm(eq, a_hi, b_lo) + mm(eq, a_lo, b_hi))


def dot2(eq, a, b_exact):
    a_hi, a_lo = split(a)
    return mm(eq, a_hi, b_exact) + mm(eq, a_lo, b_exact)


def xor_pairs(n, bit):
    return [(i, i ^ bit) for i in range(n)]


def all_sum(x, axis, n, radix=4):
    bit = 1
    while bit < n:
        r = min(radix, n // bit)
        vals = [x] + [lax.ppermute(x, axis, xor_pairs(n, d * bit)) for d in range(1, r)]
        while len(vals) > 1:
            vals = [vals[i] + vals[i + 1] for i in range(0, len(vals), 2)]
        x = vals[0]
        bit *= r
    return x


def mask_of(row_ids, col_ids, bad_list, footprint):
    row_hits = (
        (row_ids[None, :] >= bad_list[:, 0:1]) & (row_ids[None, :] < bad_list[:, 1:2])
    ).astype(f32)
    col_hits = (
        (col_ids[None, :] >= bad_list[:, 2:3]) & (col_ids[None, :] < bad_list[:, 3:4])
    ).astype(f32)
    covered = jnp.dot(row_hits.T, col_hits, preferred_element_type=f32)
    inside_rows = ((row_ids >= footprint[0]) & (row_ids < footprint[1])).astype(f32)
    inside_cols = ((col_ids >= footprint[2]) & (col_ids < footprint[3])).astype(f32)
    return (
        jnp.where(covered > 0.5, 0.0, 1.0).astype(f32)
        * inside_rows[:, None]
        * inside_cols[None, :]
    )


def local(sky_model, exposures, warp_mats, warp_blocks, psf_cols, psf_rows, bad_boxes, footprints):
    strips = lax.axis_size("strip")
    strip_index = lax.axis_index("strip")
    rows = sky_model.shape[0]
    columns = sky_model.shape[1]
    nb = columns // 128
    visits_here = warp_mats.shape[0]
    taps = psf_cols.shape[1]
    margin = taps // 2
    ext = rows + 2 * margin

    r_id = jnp.arange(rows)[:, None]
    e_id = jnp.arange(ext)[None, :]
    t_id = e_id - r_id
    row_band = sum(
        jnp.where(t_id == t, psf_rows[:, t, None, None], 0.0) for t in range(taps)
    )

    d_id = jnp.arange(3)[:, None, None] - 1
    i_id = jnp.arange(128)[None, :, None]
    o_id = jnp.arange(128)[None, None, :]
    c_t = 128 * d_id + i_id - o_id + margin
    col_band = sum(
        jnp.where(c_t == t, psf_cols[:, t, None, None, None], 0.0) for t in range(taps)
    )
    col_band_t = jnp.swapaxes(col_band, 2, 3)

    onehot = (warp_blocks[..., None] == jnp.arange(nb, dtype=jnp.int32)).astype(bf16)

    row_ids = strip_index * rows + jnp.arange(rows, dtype=jnp.int32)
    col_ids = jnp.arange(columns, dtype=jnp.int32)
    pixel_masks = jax.vmap(mask_of, in_axes=(None, None, 0, 0))(
        row_ids, col_ids, bad_boxes, footprints
    ).reshape(visits_here, rows, nb, 128)

    up = [(s, s - 1) for s in range(1, strips)]
    down = [(s, s + 1) for s in range(strips - 1)]

    def with_halo(x):
        above = lax.ppermute(x[rows - margin:], "strip", down)
        below = lax.ppermute(x[:margin], "strip", up)
        return jnp.concatenate([above, x, below], axis=0)

    def shift_blocks(y, d):
        if d == 0:
            return y
        zeros = jnp.zeros_like(y[..., :1, :])
        if d > 0:
            return jnp.concatenate([y[..., d:, :], zeros], axis=-2)
        return jnp.concatenate([zeros, y[..., :d, :]], axis=-2)

    def forward(x_ext):
        blurred_rows = dot3("vre,eji->vrji", row_band, x_ext)
        both = jnp.concatenate(split(blurred_rows), axis=1)
        pick = jax.vmap(lambda u, wb: u[:, wb])
        warped = mm("vrjki,vjkio->vrjo", pick(both, warp_blocks), warp_mats)
        warped = warped[:, :rows] + warped[:, rows:]
        out = None
        for d in range(3):
            term = dot3("vrji,vio->vrjo", shift_blocks(warped, d - 1), col_band[:, d])
            out = term if out is None else out + term
        return pixel_masks * out

    def adjoint_partial(res):
        z = res
        back = None
        for d in range(3):
            term = dot3("vrji,vio->vrjo", shift_blocks(z, 1 - d), col_band_t[:, d])
            back = term if back is None else back + term
        spread = mm("vrjo,vjkio->vrjki", jnp.concatenate(split(back), axis=1), warp_mats)
        spread = spread[:, :rows] + spread[:, rows:]
        folded = mm("vrjki,vjkb->vrbi", jnp.concatenate(split(spread), axis=1), onehot)
        folded = folded[:, :rows] + folded[:, rows:]
        return dot3("vre,vrji->eji", row_band, folded)

    visit_count = lax.axis_size("visit")
    visit_index = lax.axis_index("visit")

    def visit_sum(x):
        pieces = x.reshape(rows, visit_count, nb // visit_count, 128).swapaxes(0, 1)
        own = pieces[visit_index]
        got = []
        for d in range(1, visit_count):
            send = lax.dynamic_index_in_dim(pieces, visit_index ^ d, 0, keepdims=False)
            got.append(lax.ppermute(send, "visit", xor_pairs(visit_count, d)))
        own = (own + got[0]) + (got[1] + got[2]) if visit_count == 4 else own + sum(got)
        gathered = [own] + [
            lax.ppermute(own, "visit", xor_pairs(visit_count, d)) for d in range(1, visit_count)
        ]
        order = jnp.arange(visit_count) ^ visit_index
        full = jnp.stack(gathered)[order]
        return full.swapaxes(0, 1).reshape(rows, nb, 128)

    def reduce_partial(part):
        from_below = lax.ppermute(part[ext - margin:], "strip", down)
        from_above = lax.ppermute(part[:margin], "strip", up)
        mid = part[margin:margin + rows]
        mid = mid + jnp.concatenate(
            [from_below, jnp.zeros((rows - margin, nb, 128), f32)], axis=0
        )
        mid = mid + jnp.concatenate(
            [jnp.zeros((rows - margin, nb, 128), f32), from_above], axis=0
        )
        return visit_sum(mid)

    observed = exposures.reshape(visits_here, rows, nb, 128).astype(f32)
    start = sky_model.reshape(rows, nb, 128)
    residual = forward(with_halo(start)) - pixel_masks * observed
    gradient = with_halo(reduce_partial(adjoint_partial(residual)))
    estimate = start
    for step_index in range(STEPS):
        image_grad = forward(gradient)
        mid = gradient[margin:margin + rows]
        sums = jnp.stack(
            [
                jnp.sum(mid * mid),
                all_sum(jnp.sum(image_grad * image_grad), "visit", lax.axis_size("visit")),
            ]
        )
        grad_total, curvature = all_sum(sums, "strip", strips, radix=8)
        step_size = grad_total / curvature
        estimate = estimate - step_size * mid
        if step_index + 1 < STEPS:
            normal = with_halo(reduce_partial(adjoint_partial(image_grad)))
            gradient = gradient - step_size * normal
    return estimate.reshape(rows, columns)


def solution(mesh):
    return jax.shard_map(
        local,
        mesh=mesh,
        in_specs=(
            P("strip", None),
            P("visit", "strip", None),
            P("visit", None, None, None, None),
            P("visit", None, None),
            P("visit", None),
            P("visit", None),
            P("visit", None, None),
            P("visit", None),
        ),
        out_specs=P("strip", None),
        check_vma=False,
    )
```

```python
import jax
import jax.numpy as jnp
from jax import lax
from jax.sharding import PartitionSpec as P

STEPS = 2

f32 = jnp.float32
bf16 = jnp.bfloat16


def split(a):
    hi = lax.reduce_precision(a, exponent_bits=8, mantissa_bits=7)
    return hi.astype(bf16), (a - hi).astype(bf16)


def mm(eq, a, b):
    return jnp.einsum(eq, a, b, preferred_element_type=f32)


def dot3(eq, a, b):
    a_hi, a_lo = split(a)
    b_hi, b_lo = split(b)
    return mm(eq, a_hi, b_hi) + (mm(eq, a_hi, b_lo) + mm(eq, a_lo, b_hi))


def dot2(eq, a, b_exact):
    a_hi, a_lo = split(a)
    return mm(eq, a_hi, b_exact) + mm(eq, a_lo, b_exact)


def xor_pairs(n, bit):
    return [(i, i ^ bit) for i in range(n)]


def sum_round(x, axis, n, bit, r):
    vals = [x] + [lax.ppermute(x, axis, xor_pairs(n, d * bit)) for d in range(1, r)]
    while len(vals) > 1:
        vals = [vals[i] + vals[i + 1] for i in range(0, len(vals), 2)]
    return vals[0]


def sum_rounds(axis, n, radix):
    rounds = []
    bit = 1
    while bit < n:
        r = min(radix, n // bit)
        rounds.append((axis, n, bit, r))
        bit *= r
    return rounds


def mask_of(row_ids, col_ids, bad_list, footprint):
    row_hits = (
        (row_ids[None, :] >= bad_list[:, 0:1]) & (row_ids[None, :] < bad_list[:, 1:2])
    ).astype(f32)
    col_hits = (
        (col_ids[None, :] >= bad_list[:, 2:3]) & (col_ids[None, :] < bad_list[:, 3:4])
    ).astype(f32)
    covered = jnp.dot(row_hits.T, col_hits, preferred_element_type=f32)
    inside_rows = ((row_ids >= footprint[0]) & (row_ids < footprint[1])).astype(f32)
    inside_cols = ((col_ids >= footprint[2]) & (col_ids < footprint[3])).astype(f32)
    return (
        jnp.where(covered > 0.5, 0.0, 1.0).astype(f32)
        * inside_rows[:, None]
        * inside_cols[None, :]
    )


def local(sky_model, exposures, warp_mats, warp_blocks, psf_cols, psf_rows, bad_boxes, footprints):
    strips = lax.axis_size("strip")
    strip_index = lax.axis_index("strip")
    rows = sky_model.shape[0]
    columns = sky_model.shape[1]
    nb = columns // 128
    visits_here = warp_mats.shape[0]
    taps = psf_cols.shape[1]
    margin = taps // 2
    ext = rows + 2 * margin

    r_id = jnp.arange(rows)[:, None]
    e_id = jnp.arange(ext)[None, :]
    t_id = e_id - r_id
    row_band = sum(
        jnp.where(t_id == t, psf_rows[:, t, None, None], 0.0) for t in range(taps)
    )

    d_id = jnp.arange(3)[:, None, None] - 1
    i_id = jnp.arange(128)[None, :, None]
    o_id = jnp.arange(128)[None, None, :]
    c_t = 128 * d_id + i_id - o_id + margin
    col_band = sum(
        jnp.where(c_t == t, psf_cols[:, t, None, None, None], 0.0) for t in range(taps)
    )
    col_band_t = jnp.swapaxes(col_band, 2, 3)

    onehot = (warp_blocks[..., None] == jnp.arange(nb, dtype=jnp.int32)).astype(bf16)

    row_ids = strip_index * rows + jnp.arange(rows, dtype=jnp.int32)
    col_ids = jnp.arange(columns, dtype=jnp.int32)
    pixel_masks = jax.vmap(mask_of, in_axes=(None, None, 0, 0))(
        row_ids, col_ids, bad_boxes, footprints
    ).reshape(visits_here, rows, nb, 128)

    up = [(s, s - 1) for s in range(1, strips)]
    down = [(s, s + 1) for s in range(strips - 1)]

    def with_halo(x):
        above = lax.ppermute(x[rows - margin:], "strip", down)
        below = lax.ppermute(x[:margin], "strip", up)
        return jnp.concatenate([above, x, below], axis=0)

    def shift_blocks(y, d):
        if d == 0:
            return y
        zeros = jnp.zeros_like(y[..., :1, :])
        if d > 0:
            return jnp.concatenate([y[..., d:, :], zeros], axis=-2)
        return jnp.concatenate([zeros, y[..., :d, :]], axis=-2)

    def forward(x_ext):
        blurred_rows = dot3("vre,eji->vrji", row_band, x_ext)
        both = jnp.concatenate(split(blurred_rows), axis=1)
        pick = jax.vmap(lambda u, wb: u[:, wb])
        warped = mm("vrjki,vjkio->vrjo", pick(both, warp_blocks), warp_mats)
        warped = warped[:, :rows] + warped[:, rows:]
        out = None
        for d in range(3):
            term = dot3("vrji,vio->vrjo", shift_blocks(warped, d - 1), col_band[:, d])
            out = term if out is None else out + term
        return pixel_masks * out

    def col_adjoint(z):
        back = None
        for d in range(3):
            term = dot3("vrji,vio->vrjo", shift_blocks(z, 1 - d), col_band_t[:, d])
            back = term if back is None else back + term
        return back

    def warp_adjoint(back):
        spread = mm("vrjo,vjkio->vrjki", jnp.concatenate(split(back), axis=1), warp_mats)
        return spread[:, :rows] + spread[:, rows:]

    def fold_blocks(spread):
        folded = mm("vrjki,vjkb->vrbi", jnp.concatenate(split(spread), axis=1), onehot)
        return folded[:, :rows] + folded[:, rows:]

    def row_adjoint(folded):
        return dot3("vre,vrji->eji", row_band, folded)

    def adjoint_partial(res, scalar=None, rounds=()):
        x = res
        for k, stage in enumerate((col_adjoint, warp_adjoint, fold_blocks, row_adjoint)):
            if k < len(rounds):
                scalar = rounds[k](scalar)
            x = stage(x)
            if k < len(rounds):
                x, scalar = lax.optimization_barrier((x, scalar))
        return x, scalar

    visit_count = lax.axis_size("visit")
    visit_index = lax.axis_index("visit")

    def visit_sum(x):
        pieces = x.reshape(rows, visit_count, nb // visit_count, 128).swapaxes(0, 1)
        own = pieces[visit_index]
        got = []
        for d in range(1, visit_count):
            send = lax.dynamic_index_in_dim(pieces, visit_index ^ d, 0, keepdims=False)
            got.append(lax.ppermute(send, "visit", xor_pairs(visit_count, d)))
        own = (own + got[0]) + (got[1] + got[2]) if visit_count == 4 else own + sum(got)
        gathered = [own] + [
            lax.ppermute(own, "visit", xor_pairs(visit_count, d)) for d in range(1, visit_count)
        ]
        order = jnp.arange(visit_count) ^ visit_index
        full = jnp.stack(gathered)[order]
        return full.swapaxes(0, 1).reshape(rows, nb, 128)

    def reduce_partial(part):
        from_below = lax.ppermute(part[ext - margin:], "strip", down)
        from_above = lax.ppermute(part[:margin], "strip", up)
        mid = part[margin:margin + rows]
        mid = mid + jnp.concatenate(
            [from_below, jnp.zeros((rows - margin, nb, 128), f32)], axis=0
        )
        mid = mid + jnp.concatenate(
            [jnp.zeros((rows - margin, nb, 128), f32), from_above], axis=0
        )
        return visit_sum(mid)

    observed = exposures.reshape(visits_here, rows, nb, 128).astype(f32)
    start = sky_model.reshape(rows, nb, 128)
    residual = forward(with_halo(start)) - pixel_masks * observed
    gradient = with_halo(reduce_partial(adjoint_partial(residual)[0]))

    def visit_round(pair):
        return jnp.stack([pair[0], sum_round(pair[1], "visit", visit_count, 1, visit_count)])

    rounds = [visit_round] + [
        (lambda pair, spec=spec: sum_round(pair, *spec)) for spec in sum_rounds("strip", strips, 8)
    ]
    estimate = start
    for step_index in range(STEPS):
        image_grad = forward(gradient)
        mid = gradient[margin:margin + rows]
        sums = jnp.stack([jnp.sum(mid * mid), jnp.sum(image_grad * image_grad)])
        if step_index + 1 < STEPS:
            normal, sums = adjoint_partial(image_grad, sums, rounds)
            for rnd in rounds[4:]:
                sums = rnd(sums)
        else:
            for rnd in rounds:
                sums = rnd(sums)
        step_size = sums[0] / sums[1]
        estimate = estimate - step_size * mid
        if step_index + 1 < STEPS:
            gradient = gradient - step_size * with_halo(reduce_partial(normal))
    return estimate.reshape(rows, columns)


def solution(mesh):
    return jax.shard_map(
        local,
        mesh=mesh,
        in_specs=(
            P("strip", None),
            P("visit", "strip", None),
            P("visit", None, None, None, None),
            P("visit", None, None),
            P("visit", None),
            P("visit", None),
            P("visit", None, None),
            P("visit", None),
        ),
        out_specs=P("strip", None),
        check_vma=False,
    )
```

```python
import jax
import jax.numpy as jnp
from jax import lax
from jax.sharding import PartitionSpec as P

STEPS = 2

f32 = jnp.float32
bf16 = jnp.bfloat16


def split(a):
    hi = lax.reduce_precision(a, exponent_bits=8, mantissa_bits=7)
    return hi.astype(bf16), (a - hi).astype(bf16)


def mm(eq, a, b):
    return jnp.einsum(eq, a, b, preferred_element_type=f32)


def dot3(eq, a, b):
    a_hi, a_lo = split(a)
    b_hi, b_lo = split(b)
    return mm(eq, a_hi, b_hi) + (mm(eq, a_hi, b_lo) + mm(eq, a_lo, b_hi))


def dot2(eq, a, b_exact):
    a_hi, a_lo = split(a)
    return mm(eq, a_hi, b_exact) + mm(eq, a_lo, b_exact)


def xor_pairs(n, bit):
    return [(i, i ^ bit) for i in range(n)]


def all_sum(x, axis, n, radix=4):
    bit = 1
    while bit < n:
        r = min(radix, n // bit)
        vals = [x] + [lax.ppermute(x, axis, xor_pairs(n, d * bit)) for d in range(1, r)]
        while len(vals) > 1:
            vals = [vals[i] + vals[i + 1] for i in range(0, len(vals), 2)]
        x = vals[0]
        bit *= r
    return x


def group_round(x, axes, n, masks):
    vals = [x] + [lax.ppermute(x, axes, [(i, i ^ m) for i in range(n)]) for m in masks[1:]]
    while len(vals) > 1:
        vals = [vals[i] + vals[i + 1] for i in range(0, len(vals), 2)]
    return vals[0]


def mask_of(row_ids, col_ids, bad_list, footprint):
    row_hits = (
        (row_ids[None, :] >= bad_list[:, 0:1]) & (row_ids[None, :] < bad_list[:, 1:2])
    ).astype(f32)
    col_hits = (
        (col_ids[None, :] >= bad_list[:, 2:3]) & (col_ids[None, :] < bad_list[:, 3:4])
    ).astype(f32)
    covered = jnp.dot(row_hits.T, col_hits, preferred_element_type=f32)
    inside_rows = ((row_ids >= footprint[0]) & (row_ids < footprint[1])).astype(f32)
    inside_cols = ((col_ids >= footprint[2]) & (col_ids < footprint[3])).astype(f32)
    return (
        jnp.where(covered > 0.5, 0.0, 1.0).astype(f32)
        * inside_rows[:, None]
        * inside_cols[None, :]
    )


def local(sky_model, exposures, warp_mats, warp_blocks, psf_cols, psf_rows, bad_boxes, footprints):
    strips = lax.axis_size("strip")
    strip_index = lax.axis_index("strip")
    rows = sky_model.shape[0]
    columns = sky_model.shape[1]
    nb = columns // 128
    visits_here = warp_mats.shape[0]
    taps = psf_cols.shape[1]
    margin = taps // 2
    ext = rows + 2 * margin

    r_id = jnp.arange(rows)[:, None]
    e_id = jnp.arange(ext)[None, :]
    t_id = e_id - r_id
    row_band = sum(
        jnp.where(t_id == t, psf_rows[:, t, None, None], 0.0) for t in range(taps)
    )

    d_id = jnp.arange(3)[:, None, None] - 1
    i_id = jnp.arange(128)[None, :, None]
    o_id = jnp.arange(128)[None, None, :]
    c_t = 128 * d_id + i_id - o_id + margin
    col_band = sum(
        jnp.where(c_t == t, psf_cols[:, t, None, None, None], 0.0) for t in range(taps)
    )
    col_band_t = jnp.swapaxes(col_band, 2, 3)

    onehot = (warp_blocks[..., None] == jnp.arange(nb, dtype=jnp.int32)).astype(bf16)

    row_ids = strip_index * rows + jnp.arange(rows, dtype=jnp.int32)
    col_ids = jnp.arange(columns, dtype=jnp.int32)
    pixel_masks = jax.vmap(mask_of, in_axes=(None, None, 0, 0))(
        row_ids, col_ids, bad_boxes, footprints
    ).reshape(visits_here, rows, nb, 128)

    up = [(s, s - 1) for s in range(1, strips)]
    down = [(s, s + 1) for s in range(strips - 1)]

    def with_halo(x):
        above = lax.ppermute(x[rows - margin:], "strip", down)
        below = lax.ppermute(x[:margin], "strip", up)
        return jnp.concatenate([above, x, below], axis=0)

    def shift_blocks(y, d):
        if d == 0:
            return y
        zeros = jnp.zeros_like(y[..., :1, :])
        if d > 0:
            return jnp.concatenate([y[..., d:, :], zeros], axis=-2)
        return jnp.concatenate([zeros, y[..., :d, :]], axis=-2)

    def forward(x_ext):
        blurred_rows = dot3("vre,eji->vrji", row_band, x_ext)
        both = jnp.concatenate(split(blurred_rows), axis=1)
        pick = jax.vmap(lambda u, wb: u[:, wb])
        warped = mm("vrjki,vjkio->vrjo", pick(both, warp_blocks), warp_mats)
        warped = warped[:, :rows] + warped[:, rows:]
        out = None
        for d in range(3):
            term = dot3("vrji,vio->vrjo", shift_blocks(warped, d - 1), col_band[:, d])
            out = term if out is None else out + term
        return pixel_masks * out

    def adjoint_partial(res):
        z = res
        back = None
        for d in range(3):
            term = dot3("vrji,vio->vrjo", shift_blocks(z, 1 - d), col_band_t[:, d])
            back = term if back is None else back + term
        spread = mm("vrjo,vjkio->vrjki", jnp.concatenate(split(back), axis=1), warp_mats)
        spread = spread[:, :rows] + spread[:, rows:]
        folded = mm("vrjki,vjkb->vrbi", jnp.concatenate(split(spread), axis=1), onehot)
        folded = folded[:, :rows] + folded[:, rows:]
        return dot3("vre,vrji->eji", row_band, folded)

    visit_count = lax.axis_size("visit")
    visit_index = lax.axis_index("visit")

    def visit_sum(x):
        pieces = x.reshape(rows, visit_count, nb // visit_count, 128).swapaxes(0, 1)
        own = pieces[visit_index]
        got = []
        for d in range(1, visit_count):
            send = lax.dynamic_index_in_dim(pieces, visit_index ^ d, 0, keepdims=False)
            got.append(lax.ppermute(send, "visit", xor_pairs(visit_count, d)))
        own = (own + got[0]) + (got[1] + got[2]) if visit_count == 4 else own + sum(got)
        gathered = [own] + [
            lax.ppermute(own, "visit", xor_pairs(visit_count, d)) for d in range(1, visit_count)
        ]
        order = jnp.arange(visit_count) ^ visit_index
        full = jnp.stack(gathered)[order]
        return full.swapaxes(0, 1).reshape(rows, nb, 128)

    def reduce_partial(part):
        from_below = lax.ppermute(part[ext - margin:], "strip", down)
        from_above = lax.ppermute(part[:margin], "strip", up)
        mid = part[margin:margin + rows]
        mid = mid + jnp.concatenate(
            [from_below, jnp.zeros((rows - margin, nb, 128), f32)], axis=0
        )
        mid = mid + jnp.concatenate(
            [jnp.zeros((rows - margin, nb, 128), f32), from_above], axis=0
        )
        return visit_sum(mid)

    observed = exposures.reshape(visits_here, rows, nb, 128).astype(f32)
    start = sky_model.reshape(rows, nb, 128)
    residual = forward(with_halo(start)) - pixel_masks * observed
    gradient = with_halo(reduce_partial(adjoint_partial(residual)))
    estimate = start
    for step_index in range(STEPS):
        image_grad = forward(gradient)
        mid = gradient[margin:margin + rows]
        sums = jnp.stack([jnp.sum(mid * mid) / visit_count, jnp.sum(image_grad * image_grad)])
        low = min(8, strips)
        devices = strips * visit_count
        sums = group_round(sums, ("strip", "visit"), devices, [c * visit_count for c in range(low)])
        high = [
            (c % visit_count) | ((c // visit_count) * low * visit_count)
            for c in range(visit_count * (strips // low))
        ]
        grad_total, curvature = group_round(sums, ("strip", "visit"), devices, high)
        step_size = grad_total / curvature
        estimate = estimate - step_size * mid
        if step_index + 1 < STEPS:
            normal = with_halo(reduce_partial(adjoint_partial(image_grad)))
            gradient = gradient - step_size * normal
    return estimate.reshape(rows, columns)


def solution(mesh):
    return jax.shard_map(
        local,
        mesh=mesh,
        in_specs=(
            P("strip", None),
            P("visit", "strip", None),
            P("visit", None, None, None, None),
            P("visit", None, None),
            P("visit", None),
            P("visit", None),
            P("visit", None, None),
            P("visit", None),
        ),
        out_specs=P("strip", None),
        check_vma=False,
    )
```

```python
import jax
import jax.numpy as jnp
from jax import lax
from jax.sharding import PartitionSpec as P

STEPS = 2

f32 = jnp.float32
bf16 = jnp.bfloat16


def split(a):
    hi = lax.reduce_precision(a, exponent_bits=8, mantissa_bits=7)
    return hi.astype(bf16), (a - hi).astype(bf16)


def mm(eq, a, b):
    return jnp.einsum(eq, a, b, preferred_element_type=f32)


def dot3(eq, a, b):
    a_hi, a_lo = split(a)
    b_hi, b_lo = split(b)
    return mm(eq, a_hi, b_hi) + (mm(eq, a_hi, b_lo) + mm(eq, a_lo, b_hi))


def dot2(eq, a, b_exact):
    a_hi, a_lo = split(a)
    return mm(eq, a_hi, b_exact) + mm(eq, a_lo, b_exact)


def xor_pairs(n, bit):
    return [(i, i ^ bit) for i in range(n)]


def all_sum(x, axis, n, radix=4):
    bit = 1
    while bit < n:
        r = min(radix, n // bit)
        vals = [x] + [lax.ppermute(x, axis, xor_pairs(n, d * bit)) for d in range(1, r)]
        while len(vals) > 1:
            vals = [vals[i] + vals[i + 1] for i in range(0, len(vals), 2)]
        x = vals[0]
        bit *= r
    return x


def mask_of(row_ids, col_ids, bad_list, footprint):
    row_hits = (
        (row_ids[None, :] >= bad_list[:, 0:1]) & (row_ids[None, :] < bad_list[:, 1:2])
    ).astype(f32)
    col_hits = (
        (col_ids[None, :] >= bad_list[:, 2:3]) & (col_ids[None, :] < bad_list[:, 3:4])
    ).astype(f32)
    covered = jnp.dot(row_hits.T, col_hits, preferred_element_type=f32)
    inside_rows = ((row_ids >= footprint[0]) & (row_ids < footprint[1])).astype(f32)
    inside_cols = ((col_ids >= footprint[2]) & (col_ids < footprint[3])).astype(f32)
    return (
        jnp.where(covered > 0.5, 0.0, 1.0).astype(f32)
        * inside_rows[:, None]
        * inside_cols[None, :]
    )


def local(sky_model, exposures, warp_mats, warp_blocks, psf_cols, psf_rows, bad_boxes, footprints):
    strips = lax.axis_size("strip")
    strip_index = lax.axis_index("strip")
    rows = sky_model.shape[0]
    columns = sky_model.shape[1]
    nb = columns // 128
    visits_here = warp_mats.shape[0]
    taps = psf_cols.shape[1]
    margin = taps // 2
    ext = rows + 2 * margin

    r_id = jnp.arange(rows)[:, None]
    e_id = jnp.arange(ext)[None, :]
    t_id = e_id - r_id
    row_band = sum(
        jnp.where(t_id == t, psf_rows[:, t, None, None], 0.0) for t in range(taps)
    )

    d_id = jnp.arange(3)[:, None, None] - 1
    i_id = jnp.arange(128)[None, :, None]
    o_id = jnp.arange(128)[None, None, :]
    c_t = 128 * d_id + i_id - o_id + margin
    col_band = sum(
        jnp.where(c_t == t, psf_cols[:, t, None, None, None], 0.0) for t in range(taps)
    )
    col_band_t = jnp.swapaxes(col_band, 2, 3)

    onehot = (warp_blocks[..., None] == jnp.arange(nb, dtype=jnp.int32)).astype(bf16)

    row_ids = strip_index * rows + jnp.arange(rows, dtype=jnp.int32)
    col_ids = jnp.arange(columns, dtype=jnp.int32)
    pixel_masks = jax.vmap(mask_of, in_axes=(None, None, 0, 0))(
        row_ids, col_ids, bad_boxes, footprints
    ).reshape(visits_here, rows, nb, 128)

    up = [(s, s - 1) for s in range(1, strips)]
    down = [(s, s + 1) for s in range(strips - 1)]

    def with_halo(x):
        above = lax.ppermute(x[rows - margin:], "strip", down)
        below = lax.ppermute(x[:margin], "strip", up)
        return jnp.concatenate([above, x, below], axis=0)

    def shift_blocks(y, d):
        if d == 0:
            return y
        zeros = jnp.zeros_like(y[..., :1, :])
        if d > 0:
            return jnp.concatenate([y[..., d:, :], zeros], axis=-2)
        return jnp.concatenate([zeros, y[..., :d, :]], axis=-2)

    def forward(x_ext):
        blurred_rows = dot3("vre,eji->vrji", row_band, x_ext)
        both = jnp.concatenate(split(blurred_rows), axis=1)
        pick = jax.vmap(lambda u, wb: u[:, wb])
        warped = mm("vrjki,vjkio->vrjo", pick(both, warp_blocks), warp_mats)
        warped = warped[:, :rows] + warped[:, rows:]
        out = None
        for d in range(3):
            term = dot3("vrji,vio->vrjo", shift_blocks(warped, d - 1), col_band[:, d])
            out = term if out is None else out + term
        return pixel_masks * out

    def adjoint_partial(res):
        z = res
        back = None
        for d in range(3):
            term = dot3("vrji,vio->vrjo", shift_blocks(z, 1 - d), col_band_t[:, d])
            back = term if back is None else back + term
        spread = mm("vrjo,vjkio->vrjki", jnp.concatenate(split(back), axis=1), warp_mats)
        spread = spread[:, :rows] + spread[:, rows:]
        folded = mm("vrjki,vjkb->vrbi", jnp.concatenate(split(spread), axis=1), onehot)
        folded = folded[:, :rows] + folded[:, rows:]
        return dot3("vre,vrji->eji", row_band, folded)

    visit_count = lax.axis_size("visit")
    visit_index = lax.axis_index("visit")

    def visit_sum(x):
        pieces = x.reshape(rows, visit_count, nb // visit_count, 128).swapaxes(0, 1)
        own = pieces[visit_index]
        got = []
        for d in range(1, visit_count):
            send = lax.dynamic_index_in_dim(pieces, visit_index ^ d, 0, keepdims=False)
            got.append(lax.ppermute(send, "visit", xor_pairs(visit_count, d)))
        own = (own + got[0]) + (got[1] + got[2]) if visit_count == 4 else own + sum(got)
        gathered = [own] + [
            lax.ppermute(own, "visit", xor_pairs(visit_count, d)) for d in range(1, visit_count)
        ]
        order = jnp.arange(visit_count) ^ visit_index
        full = jnp.stack(gathered)[order]
        return full.swapaxes(0, 1).reshape(rows, nb, 128)

    def reduce_partial(part):
        from_below = lax.ppermute(part[ext - margin:], "strip", down)
        from_above = lax.ppermute(part[:margin], "strip", up)
        mid = part[margin:margin + rows]
        mid = mid + jnp.concatenate(
            [from_below, jnp.zeros((rows - margin, nb, 128), f32)], axis=0
        )
        mid = mid + jnp.concatenate(
            [jnp.zeros((rows - margin, nb, 128), f32), from_above], axis=0
        )
        return visit_sum(mid)

    observed = exposures.reshape(visits_here, rows, nb, 128).astype(f32)
    start = sky_model.reshape(rows, nb, 128)
    residual = forward(with_halo(start)) - pixel_masks * observed
    gradient = with_halo(reduce_partial(adjoint_partial(residual)))
    estimate = start
    for step_index in range(STEPS):
        image_grad = forward(gradient)
        mid = gradient[margin:margin + rows]
        sums = jnp.stack(
            [
                jnp.sum(mid * mid),
                all_sum(jnp.sum(image_grad * image_grad), "visit", lax.axis_size("visit")),
            ]
        )
        grad_total, curvature = all_sum(sums, "strip", strips)
        step_size = grad_total / curvature
        estimate = estimate - step_size * mid
        if step_index + 1 < STEPS:
            normal = with_halo(reduce_partial(adjoint_partial(image_grad)))
            gradient = gradient - step_size * normal
    return estimate.reshape(rows, columns)


def solution(mesh):
    return jax.shard_map(
        local,
        mesh=mesh,
        in_specs=(
            P("strip", None),
            P("visit", "strip", None),
            P("visit", None, None, None, None),
            P("visit", None, None),
            P("visit", None),
            P("visit", None),
            P("visit", None, None),
            P("visit", None),
        ),
        out_specs=P("strip", None),
        check_vma=False,
    )
```

```python
import jax
import jax.numpy as jnp
from jax import lax
from jax.sharding import PartitionSpec as P

STEPS = 2

f32 = jnp.float32
bf16 = jnp.bfloat16


def split(a):
    hi = lax.reduce_precision(a, exponent_bits=8, mantissa_bits=7)
    return hi.astype(bf16), (a - hi).astype(bf16)


def mm(eq, a, b):
    return jnp.einsum(eq, a, b, preferred_element_type=f32)


def dot3(eq, a, b):
    a_hi, a_lo = split(a)
    b_hi, b_lo = split(b)
    return mm(eq, a_hi, b_hi) + (mm(eq, a_hi, b_lo) + mm(eq, a_lo, b_hi))


def dot2(eq, a, b_exact):
    a_hi, a_lo = split(a)
    return mm(eq, a_hi, b_exact) + mm(eq, a_lo, b_exact)


def xor_pairs(n, bit):
    return [(i, i ^ bit) for i in range(n)]


def all_sum(x, axis, n, radix=4):
    bit = 1
    while bit < n:
        r = min(radix, n // bit)
        vals = [x] + [lax.ppermute(x, axis, xor_pairs(n, d * bit)) for d in range(1, r)]
        while len(vals) > 1:
            vals = [vals[i] + vals[i + 1] for i in range(0, len(vals), 2)]
        x = vals[0]
        bit *= r
    return x


def mask_of(row_ids, col_ids, bad_list, footprint):
    row_hits = (
        (row_ids[None, :] >= bad_list[:, 0:1]) & (row_ids[None, :] < bad_list[:, 1:2])
    ).astype(f32)
    col_hits = (
        (col_ids[None, :] >= bad_list[:, 2:3]) & (col_ids[None, :] < bad_list[:, 3:4])
    ).astype(f32)
    covered = jnp.dot(row_hits.T, col_hits, preferred_element_type=f32)
    inside_rows = ((row_ids >= footprint[0]) & (row_ids < footprint[1])).astype(f32)
    inside_cols = ((col_ids >= footprint[2]) & (col_ids < footprint[3])).astype(f32)
    return (
        jnp.where(covered > 0.5, 0.0, 1.0).astype(f32)
        * inside_rows[:, None]
        * inside_cols[None, :]
    )


def local(sky_model, exposures, warp_mats, warp_blocks, psf_cols, psf_rows, bad_boxes, footprints):
    strips = lax.axis_size("strip")
    strip_index = lax.axis_index("strip")
    rows = sky_model.shape[0]
    columns = sky_model.shape[1]
    nb = columns // 128
    visits_here = warp_mats.shape[0]
    taps = psf_cols.shape[1]
    margin = taps // 2
    ext = rows + 2 * margin

    r_id = jnp.arange(rows)[:, None]
    e_id = jnp.arange(ext)[None, :]
    t_id = e_id - r_id
    row_band = sum(
        jnp.where(t_id == t, psf_rows[:, t, None, None], 0.0) for t in range(taps)
    )

    d_id = jnp.arange(3)[:, None, None] - 1
    i_id = jnp.arange(128)[None, :, None]
    o_id = jnp.arange(128)[None, None, :]
    c_t = 128 * d_id + i_id - o_id + margin
    col_band = sum(
        jnp.where(c_t == t, psf_cols[:, t, None, None, None], 0.0) for t in range(taps)
    )
    col_band_t = jnp.swapaxes(col_band, 2, 3)

    onehot = (warp_blocks[..., None] == jnp.arange(nb, dtype=jnp.int32)).astype(bf16)

    row_ids = strip_index * rows + jnp.arange(rows, dtype=jnp.int32)
    col_ids = jnp.arange(columns, dtype=jnp.int32)
    pixel_masks = jax.vmap(mask_of, in_axes=(None, None, 0, 0))(
        row_ids, col_ids, bad_boxes, footprints
    ).reshape(visits_here, rows, nb, 128)

    up = [(s, s - 1) for s in range(1, strips)]
    down = [(s, s + 1) for s in range(strips - 1)]

    def with_halo(x):
        above = lax.ppermute(x[rows - margin:], "strip", down)
        below = lax.ppermute(x[:margin], "strip", up)
        return jnp.concatenate([above, x, below], axis=0)

    def shift_blocks(y, d):
        if d == 0:
            return y
        zeros = jnp.zeros_like(y[..., :1, :])
        if d > 0:
            return jnp.concatenate([y[..., d:, :], zeros], axis=-2)
        return jnp.concatenate([zeros, y[..., :d, :]], axis=-2)

    def forward(x_ext):
        blurred_rows = dot3("vre,eji->vrji", row_band, x_ext)
        both = jnp.concatenate(split(blurred_rows), axis=1)
        pick = jax.vmap(lambda u, wb: u[:, wb])
        warped = mm("vrjki,vjkio->vrjo", pick(both, warp_blocks), warp_mats)
        warped = warped[:, :rows] + warped[:, rows:]
        out = None
        for d in range(3):
            term = dot3("vrji,vio->vrjo", shift_blocks(warped, d - 1), col_band[:, d])
            out = term if out is None else out + term
        return pixel_masks * out

    def adjoint_partial(res):
        z = res
        back = None
        for d in range(3):
            term = dot3("vrji,vio->vrjo", shift_blocks(z, 1 - d), col_band_t[:, d])
            back = term if back is None else back + term
        spread = mm("vrjo,vjkio->vrjki", jnp.concatenate(split(back), axis=1), warp_mats)
        spread = spread[:, :rows] + spread[:, rows:]
        folded = mm("vrjki,vjkb->vrbi", jnp.concatenate(split(spread), axis=1), onehot)
        folded = folded[:, :rows] + folded[:, rows:]
        return dot3("vre,vrji->eji", row_band, folded)

    visit_count = lax.axis_size("visit")
    visit_index = lax.axis_index("visit")

    def visit_sum(x):
        pieces = x.reshape(rows, visit_count, nb // visit_count, 128).swapaxes(0, 1)
        own = pieces[visit_index]
        got = []
        for d in range(1, visit_count):
            send = lax.dynamic_index_in_dim(pieces, visit_index ^ d, 0, keepdims=False)
            got.append(lax.ppermute(send, "visit", xor_pairs(visit_count, d)))
        own = (own + got[0]) + (got[1] + got[2]) if visit_count == 4 else own + sum(got)
        gathered = [own] + [
            lax.ppermute(own, "visit", xor_pairs(visit_count, d)) for d in range(1, visit_count)
        ]
        order = jnp.arange(visit_count) ^ visit_index
        full = jnp.stack(gathered)[order]
        return full.swapaxes(0, 1).reshape(rows, nb, 128)

    def reduce_partial(part):
        from_below = lax.ppermute(part[ext - margin:], "strip", down)
        from_above = lax.ppermute(part[:margin], "strip", up)
        mid = part[margin:margin + rows]
        mid = mid + jnp.concatenate(
            [from_below, jnp.zeros((rows - margin, nb, 128), f32)], axis=0
        )
        mid = mid + jnp.concatenate(
            [jnp.zeros((rows - margin, nb, 128), f32), from_above], axis=0
        )
        return visit_sum(mid)

    observed = exposures.reshape(visits_here, rows, nb, 128).astype(f32)
    start = sky_model.reshape(rows, nb, 128)
    residual = forward(with_halo(start)) - pixel_masks * observed
    gradient = with_halo(reduce_partial(adjoint_partial(residual)))
    estimate = start
    for step_index in range(STEPS):
        image_grad = forward(gradient)
        mid = gradient[margin:margin + rows]
        sums = jnp.stack(
            [
                jnp.sum(mid * mid),
                all_sum(jnp.sum(image_grad * image_grad), "visit", lax.axis_size("visit"), radix=2),
            ]
        )
        grad_total, curvature = all_sum(sums, "strip", strips, radix=2)
        step_size = grad_total / curvature
        estimate = estimate - step_size * mid
        if step_index + 1 < STEPS:
            normal = with_halo(reduce_partial(adjoint_partial(image_grad)))
            gradient = gradient - step_size * normal
    return estimate.reshape(rows, columns)


def solution(mesh):
    return jax.shard_map(
        local,
        mesh=mesh,
        in_specs=(
            P("strip", None),
            P("visit", "strip", None),
            P("visit", None, None, None, None),
            P("visit", None, None),
            P("visit", None),
            P("visit", None),
            P("visit", None, None),
            P("visit", None),
        ),
        out_specs=P("strip", None),
        check_vma=False,
    )
```

```python
import jax
import jax.numpy as jnp
from jax import lax
from jax.sharding import PartitionSpec as P

STEPS = 2

f32 = jnp.float32
bf16 = jnp.bfloat16


def split(a):
    hi = lax.reduce_precision(a, exponent_bits=8, mantissa_bits=7)
    return hi.astype(bf16), (a - hi).astype(bf16)


def mm(eq, a, b):
    return jnp.einsum(eq, a, b, preferred_element_type=f32)


def dot3(eq, a, b):
    a_hi, a_lo = split(a)
    b_hi, b_lo = split(b)
    return mm(eq, a_hi, b_hi) + (mm(eq, a_hi, b_lo) + mm(eq, a_lo, b_hi))


def dot2(eq, a, b_exact):
    a_hi, a_lo = split(a)
    return mm(eq, a_hi, b_exact) + mm(eq, a_lo, b_exact)


def xor_pairs(n, bit):
    return [(i, i ^ bit) for i in range(n)]


def all_sum(x, axis, n, radix=4):
    bit = 1
    while bit < n:
        r = min(radix, n // bit)
        vals = [x] + [lax.ppermute(x, axis, xor_pairs(n, d * bit)) for d in range(1, r)]
        while len(vals) > 1:
            vals = [vals[i] + vals[i + 1] for i in range(0, len(vals), 2)]
        x = vals[0]
        bit *= r
    return x


def mask_of(row_ids, col_ids, bad_list, footprint):
    row_hits = (
        (row_ids[None, :] >= bad_list[:, 0:1]) & (row_ids[None, :] < bad_list[:, 1:2])
    ).astype(f32)
    col_hits = (
        (col_ids[None, :] >= bad_list[:, 2:3]) & (col_ids[None, :] < bad_list[:, 3:4])
    ).astype(f32)
    covered = jnp.dot(row_hits.T, col_hits, preferred_element_type=f32)
    inside_rows = ((row_ids >= footprint[0]) & (row_ids < footprint[1])).astype(f32)
    inside_cols = ((col_ids >= footprint[2]) & (col_ids < footprint[3])).astype(f32)
    return (
        jnp.where(covered > 0.5, 0.0, 1.0).astype(f32)
        * inside_rows[:, None]
        * inside_cols[None, :]
    )


def local(sky_model, exposures, warp_mats, warp_blocks, psf_cols, psf_rows, bad_boxes, footprints):
    strips = lax.axis_size("strip")
    strip_index = lax.axis_index("strip")
    rows = sky_model.shape[0]
    columns = sky_model.shape[1]
    nb = columns // 128
    visits_here = warp_mats.shape[0]
    taps = psf_cols.shape[1]
    margin = taps // 2
    ext = rows + 2 * margin

    r_id = jnp.arange(rows)[:, None]
    e_id = jnp.arange(ext)[None, :]
    t_id = e_id - r_id
    row_band = sum(
        jnp.where(t_id == t, psf_rows[:, t, None, None], 0.0) for t in range(taps)
    )

    d_id = jnp.arange(3)[:, None, None] - 1
    i_id = jnp.arange(128)[None, :, None]
    o_id = jnp.arange(128)[None, None, :]
    c_t = 128 * d_id + i_id - o_id + margin
    col_band = sum(
        jnp.where(c_t == t, psf_cols[:, t, None, None, None], 0.0) for t in range(taps)
    )

    onehot = (warp_blocks[..., None] == jnp.arange(nb, dtype=jnp.int32)).astype(bf16)

    row_ids = strip_index * rows + jnp.arange(rows, dtype=jnp.int32)
    col_ids = jnp.arange(columns, dtype=jnp.int32)
    pixel_masks = jax.vmap(mask_of, in_axes=(None, None, 0, 0))(
        row_ids, col_ids, bad_boxes, footprints
    ).reshape(visits_here, rows, nb, 128)

    up = [(s, s - 1) for s in range(1, strips)]
    down = [(s, s + 1) for s in range(strips - 1)]

    def with_halo(x):
        above = lax.ppermute(x[rows - margin:], "strip", down)
        below = lax.ppermute(x[:margin], "strip", up)
        return jnp.concatenate([above, x, below], axis=0)

    def shift_blocks(y, d):
        if d == 0:
            return y
        zeros = jnp.zeros_like(y[..., :1, :])
        if d > 0:
            return jnp.concatenate([y[..., d:, :], zeros], axis=-2)
        return jnp.concatenate([zeros, y[..., :d, :]], axis=-2)

    def forward(x_ext):
        blurred_rows = dot3("vre,eji->vrji", row_band, x_ext)
        both = jnp.concatenate(split(blurred_rows), axis=1)
        pick = jax.vmap(lambda u, wb: u[:, wb])
        warped = mm("vrjki,vjkio->vrjo", pick(both, warp_blocks), warp_mats)
        warped = warped[:, :rows] + warped[:, rows:]
        out = None
        for d in range(3):
            term = dot3("vrji,vio->vrjo", shift_blocks(warped, d - 1), col_band[:, d])
            out = term if out is None else out + term
        return pixel_masks * out

    def adjoint_partial(res):
        z = res
        back = None
        for d in range(3):
            term = dot3("vrjo,vio->vrji", shift_blocks(z, 1 - d), col_band[:, d])
            back = term if back is None else back + term
        spread = mm("vrjo,vjkio->vrjki", jnp.concatenate(split(back), axis=1), warp_mats)
        spread = spread[:, :rows] + spread[:, rows:]
        folded = mm("vrjki,vjkb->vrbi", jnp.concatenate(split(spread), axis=1), onehot)
        folded = folded[:, :rows] + folded[:, rows:]
        return dot3("vre,vrji->eji", row_band, folded)

    visit_count = lax.axis_size("visit")
    visit_index = lax.axis_index("visit")

    def visit_sum(x):
        pieces = x.reshape(rows, visit_count, nb // visit_count, 128).swapaxes(0, 1)
        own = pieces[visit_index]
        got = []
        for d in range(1, visit_count):
            send = lax.dynamic_index_in_dim(pieces, visit_index ^ d, 0, keepdims=False)
            got.append(lax.ppermute(send, "visit", xor_pairs(visit_count, d)))
        own = (own + got[0]) + (got[1] + got[2]) if visit_count == 4 else own + sum(got)
        gathered = [own] + [
            lax.ppermute(own, "visit", xor_pairs(visit_count, d)) for d in range(1, visit_count)
        ]
        order = jnp.arange(visit_count) ^ visit_index
        full = jnp.stack(gathered)[order]
        return full.swapaxes(0, 1).reshape(rows, nb, 128)

    def reduce_partial(part):
        from_below = lax.ppermute(part[ext - margin:], "strip", down)
        from_above = lax.ppermute(part[:margin], "strip", up)
        mid = part[margin:margin + rows]
        mid = mid + jnp.concatenate(
            [from_below, jnp.zeros((rows - margin, nb, 128), f32)], axis=0
        )
        mid = mid + jnp.concatenate(
            [jnp.zeros((rows - margin, nb, 128), f32), from_above], axis=0
        )
        return visit_sum(mid)

    observed = exposures.reshape(visits_here, rows, nb, 128).astype(f32)
    start = sky_model.reshape(rows, nb, 128)
    residual = forward(with_halo(start)) - pixel_masks * observed
    gradient = with_halo(reduce_partial(adjoint_partial(residual)))
    estimate = start
    for step_index in range(STEPS):
        image_grad = forward(gradient)
        mid = gradient[margin:margin + rows]
        sums = jnp.stack(
            [
                jnp.sum(mid * mid),
                all_sum(jnp.sum(image_grad * image_grad), "visit", lax.axis_size("visit")),
            ]
        )
        grad_total, curvature = all_sum(sums, "strip", strips)
        step_size = grad_total / curvature
        estimate = estimate - step_size * mid
        if step_index + 1 < STEPS:
            normal = with_halo(reduce_partial(adjoint_partial(image_grad)))
            gradient = gradient - step_size * normal
    return estimate.reshape(rows, columns)


def solution(mesh):
    return jax.shard_map(
        local,
        mesh=mesh,
        in_specs=(
            P("strip", None),
            P("visit", "strip", None),
            P("visit", None, None, None, None),
            P("visit", None, None),
            P("visit", None),
            P("visit", None),
            P("visit", None, None),
            P("visit", None),
        ),
        out_specs=P("strip", None),
        check_vma=False,
    )
```

```python
import jax
import jax.numpy as jnp
from jax import lax
from jax.sharding import PartitionSpec as P

STEPS = 2

f32 = jnp.float32
bf16 = jnp.bfloat16


def split(a):
    hi = lax.reduce_precision(a, exponent_bits=8, mantissa_bits=7)
    return hi.astype(bf16), (a - hi).astype(bf16)


def mm(eq, a, b):
    return jnp.einsum(eq, a, b, preferred_element_type=f32)


def dot3(eq, a, b):
    a_hi, a_lo = split(a)
    b_hi, b_lo = split(b)
    return mm(eq, a_hi, b_hi) + (mm(eq, a_hi, b_lo) + mm(eq, a_lo, b_hi))


def dot2(eq, a, b_exact):
    a_hi, a_lo = split(a)
    return mm(eq, a_hi, b_exact) + mm(eq, a_lo, b_exact)


def xor_pairs(n, bit):
    return [(i, i ^ bit) for i in range(n)]


def all_sum(x, axis, n, radix=4):
    bit = 1
    while bit < n:
        r = min(radix, n // bit)
        vals = [x] + [lax.ppermute(x, axis, xor_pairs(n, d * bit)) for d in range(1, r)]
        while len(vals) > 1:
            vals = [vals[i] + vals[i + 1] for i in range(0, len(vals), 2)]
        x = vals[0]
        bit *= r
    return x


def mask_of(row_ids, col_ids, bad_list, footprint):
    row_hits = (
        (row_ids[None, :] >= bad_list[:, 0:1]) & (row_ids[None, :] < bad_list[:, 1:2])
    ).astype(f32)
    col_hits = (
        (col_ids[None, :] >= bad_list[:, 2:3]) & (col_ids[None, :] < bad_list[:, 3:4])
    ).astype(f32)
    covered = jnp.dot(row_hits.T, col_hits, preferred_element_type=f32)
    inside_rows = ((row_ids >= footprint[0]) & (row_ids < footprint[1])).astype(f32)
    inside_cols = ((col_ids >= footprint[2]) & (col_ids < footprint[3])).astype(f32)
    return (
        jnp.where(covered > 0.5, 0.0, 1.0).astype(f32)
        * inside_rows[:, None]
        * inside_cols[None, :]
    )


def local(sky_model, exposures, warp_mats, warp_blocks, psf_cols, psf_rows, bad_boxes, footprints):
    strips = lax.axis_size("strip")
    strip_index = lax.axis_index("strip")
    rows = sky_model.shape[0]
    columns = sky_model.shape[1]
    nb = columns // 128
    visits_here = warp_mats.shape[0]
    taps = psf_cols.shape[1]
    margin = taps // 2
    ext = rows + 2 * margin

    r_id = jnp.arange(rows)[:, None]
    e_id = jnp.arange(ext)[None, :]
    t_id = e_id - r_id
    row_band = sum(
        jnp.where(t_id == t, psf_rows[:, t, None, None], 0.0) for t in range(taps)
    )

    d_id = jnp.arange(3)[:, None, None] - 1
    i_id = jnp.arange(128)[None, :, None]
    o_id = jnp.arange(128)[None, None, :]
    c_t = 128 * d_id + i_id - o_id + margin
    col_band = sum(
        jnp.where(c_t == t, psf_cols[:, t, None, None, None], 0.0) for t in range(taps)
    )

    onehot = (warp_blocks[..., None] == jnp.arange(nb, dtype=jnp.int32)).astype(bf16)

    row_ids = strip_index * rows + jnp.arange(rows, dtype=jnp.int32)
    col_ids = jnp.arange(columns, dtype=jnp.int32)
    pixel_masks = jax.vmap(mask_of, in_axes=(None, None, 0, 0))(
        row_ids, col_ids, bad_boxes, footprints
    ).reshape(visits_here, rows, nb, 128)

    up = [(s, s - 1) for s in range(1, strips)]
    down = [(s, s + 1) for s in range(strips - 1)]

    def with_halo(x):
        above = lax.ppermute(x[rows - margin:], "strip", down)
        below = lax.ppermute(x[:margin], "strip", up)
        return jnp.concatenate([above, x, below], axis=0)

    def shift_blocks(y, d):
        if d == 0:
            return y
        zeros = jnp.zeros_like(y[..., :1, :])
        if d > 0:
            return jnp.concatenate([y[..., d:, :], zeros], axis=-2)
        return jnp.concatenate([zeros, y[..., :d, :]], axis=-2)

    def forward(x_ext):
        blurred_rows = dot3("vre,eji->vrji", row_band, x_ext)
        both = jnp.concatenate(split(blurred_rows), axis=1)
        picked = mm("vrbi,vjkb->vrjki", both, onehot).astype(bf16)
        warped = mm("vrjki,vjkio->vrjo", picked, warp_mats)
        warped = warped[:, :rows] + warped[:, rows:]
        out = None
        for d in range(3):
            term = dot3("vrji,vio->vrjo", shift_blocks(warped, d - 1), col_band[:, d])
            out = term if out is None else out + term
        return pixel_masks * out

    def adjoint_partial(res):
        z = res
        back = None
        for d in range(3):
            term = dot3("vrjo,vio->vrji", shift_blocks(z, 1 - d), col_band[:, d])
            back = term if back is None else back + term
        spread = mm("vrjo,vjkio->vrjki", jnp.concatenate(split(back), axis=1), warp_mats)
        spread = spread[:, :rows] + spread[:, rows:]
        folded = mm("vrjki,vjkb->vrbi", jnp.concatenate(split(spread), axis=1), onehot)
        folded = folded[:, :rows] + folded[:, rows:]
        return dot3("vre,vrji->eji", row_band, folded)

    visit_count = lax.axis_size("visit")
    visit_index = lax.axis_index("visit")

    def visit_sum(x):
        pieces = x.reshape(rows, visit_count, nb // visit_count, 128).swapaxes(0, 1)
        own = pieces[visit_index]
        got = []
        for d in range(1, visit_count):
            send = lax.dynamic_index_in_dim(pieces, visit_index ^ d, 0, keepdims=False)
            got.append(lax.ppermute(send, "visit", xor_pairs(visit_count, d)))
        own = (own + got[0]) + (got[1] + got[2]) if visit_count == 4 else own + sum(got)
        gathered = [own] + [
            lax.ppermute(own, "visit", xor_pairs(visit_count, d)) for d in range(1, visit_count)
        ]
        order = jnp.arange(visit_count) ^ visit_index
        full = jnp.stack(gathered)[order]
        return full.swapaxes(0, 1).reshape(rows, nb, 128)

    def reduce_partial(part):
        from_below = lax.ppermute(part[ext - margin:], "strip", down)
        from_above = lax.ppermute(part[:margin], "strip", up)
        mid = part[margin:margin + rows]
        mid = mid + jnp.concatenate(
            [from_below, jnp.zeros((rows - margin, nb, 128), f32)], axis=0
        )
        mid = mid + jnp.concatenate(
            [jnp.zeros((rows - margin, nb, 128), f32), from_above], axis=0
        )
        return visit_sum(mid)

    observed = exposures.reshape(visits_here, rows, nb, 128).astype(f32)
    start = sky_model.reshape(rows, nb, 128)
    residual = forward(with_halo(start)) - pixel_masks * observed
    gradient = with_halo(reduce_partial(adjoint_partial(residual)))
    estimate = start
    for step_index in range(STEPS):
        image_grad = forward(gradient)
        mid = gradient[margin:margin + rows]
        sums = jnp.stack(
            [
                jnp.sum(mid * mid),
                all_sum(jnp.sum(image_grad * image_grad), "visit", lax.axis_size("visit")),
            ]
        )
        grad_total, curvature = all_sum(sums, "strip", strips)
        step_size = grad_total / curvature
        estimate = estimate - step_size * mid
        if step_index + 1 < STEPS:
            normal = with_halo(reduce_partial(adjoint_partial(image_grad)))
            gradient = gradient - step_size * normal
    return estimate.reshape(rows, columns)


def solution(mesh):
    return jax.shard_map(
        local,
        mesh=mesh,
        in_specs=(
            P("strip", None),
            P("visit", "strip", None),
            P("visit", None, None, None, None),
            P("visit", None, None),
            P("visit", None),
            P("visit", None),
            P("visit", None, None),
            P("visit", None),
        ),
        out_specs=P("strip", None),
        check_vma=False,
    )
```
